128 devices in a mesh: row: 8 (over x, core), col: 16 (over z, y).
Axes of the slice: x: 4, y: 4, z: 4, core: 2. Of those that a mesh axis runs over, the one named last changes fastest.
Arguments:
- left_factor: float32 [23, 8, 128, 16, 16, 128], P(None, 'row', None, None, 'col'), may hold values from -5 to 5
- pick_site: int32 [23, 8, 128], P(None, 'row'), may hold values from 0 to 131071
- noise: float32 [23, 8, 128], P(None, 'row'), may hold values from 2 to 5
Outputs:
- panels: float32 [8, 16, 184, 2, 128], P('row', 'col')
The draws below stay inside these ranges and needn't reach their ends.
All inputs are finite; a program needn't handle non-finite values.
Results may differ from the reference program's by a relative error of at most 0.000064.
Values sent between devices are 32-bit elements; how exact they have to be, the bound alone decides.
No kernel may reach another device: no remote copies, remote signals or barrier semaphores. Data moves between devices by JAX's collectives and lax.ppermute only.
A program may use at most 128 MiB of HBM per device.

```python
import math
import jax
import jax.numpy as jnp
from jax import lax

BLOCK = 128
COL_BLOCKS = 16
ROW_BLOCKS = 23
GRID_X = 64
GRID_Y = 64
GRID_Z = 32
N_ROW = 8
N_COL = 16


def draw_left_factor(key, part):
    left_cols = COL_BLOCKS * N_COL * BLOCK
    full_shape = (ROW_BLOCKS, N_ROW, BLOCK, COL_BLOCKS, N_COL, BLOCK)
    key_base = jax.random.fold_in(key, 11)
    lead_mask = (jnp.arange(ROW_BLOCKS)[:, None] == 0) & (jnp.arange(N_ROW)[None, :] < 2)
    lead_mask = lead_mask[:, :, None, None, None, None]
    inv_root = 1.0 / math.sqrt(left_cols)
    base_draw = jax.random.truncated_normal(key_base, -4.0, 4.0, full_shape, jnp.float32)
    deep_rows = 6.0 * inv_root * base_draw
    lead_rows = 0.9 * inv_root * base_draw
    return jnp.where(lead_mask, lead_rows, deep_rows).astype(jnp.float32)


def with_ends(result, key, least, high):
    index_at = [jax.random.randint(jax.random.fold_in(key, axis), (), 0, length) for axis, length in enumerate(result.shape)]
    longest = result.shape.index(max(result.shape))
    neighbour = index_at[:longest] + [(index_at[longest] + 1) % result.shape[longest]] + index_at[longest + 1:]
    return result.at[tuple(index_at)].set(least).at[tuple(neighbour)].set(high)


def levels(own_key, dims, shards, smallest, high):
    def one(axis_at, parts):
        steps = jax.random.uniform(jax.random.fold_in(jax.random.fold_in(own_key, 6), axis_at), (parts,), jnp.float32, smallest / len(shards), high / len(shards))
        return jnp.repeat(jnp.exp(steps), dims[axis_at] // parts).reshape((-1,) + (1,) * (len(dims) - axis_at - 1))

    gain = one(*shards[0])
    for cut in shards[1:]:
        gain = gain * one(*cut)
    return gain


def setup_inputs(seed: int = 0) -> dict:
    arg_keys = jax.random.split(jax.random.key(seed), 4)
    return {
        "left_factor": draw_left_factor(jax.random.fold_in(arg_keys[3], 71), 0),
        "pick_site": with_ends(jax.random.randint(arg_keys[1], (ROW_BLOCKS, N_ROW, BLOCK), 0, GRID_X * GRID_Y * GRID_Z), jax.random.fold_in(arg_keys[1], 1), 0, (GRID_X * GRID_Y * GRID_Z) - 1).astype(jnp.int32),
        "noise": jnp.clip(jnp.exp(math.log(5.0) - 0.916290732 * jax.random.uniform(arg_keys[2], (ROW_BLOCKS, N_ROW, BLOCK), jnp.float32) ** levels(arg_keys[2], (ROW_BLOCKS, N_ROW, BLOCK), ((1, 8),), -0.2, 0.2)), 2.0, 5.0),
    }


LATERAL = 24.0
VERTICAL = 6.0

def site_coords(site_ids):
    site_ids = site_ids.astype(jnp.int32)
    coord_x = site_ids // (GRID_Y * GRID_Z)
    coord_y = site_ids // GRID_Z % GRID_Y
    coord_z = site_ids % GRID_Z
    return jnp.stack([coord_x, coord_y, coord_z]).astype(jnp.float32)

def matern(row_coords, col_coords):
    lengths = (LATERAL, LATERAL, VERTICAL)
    squared = jnp.zeros((row_coords.shape[1], col_coords.shape[1]), jnp.float32)
    for dim_index in range(3):
        difference = (row_coords[dim_index][:, None] - col_coords[dim_index][None, :]) / lengths[dim_index]
        squared = squared + difference * difference
    radius = jnp.sqrt(3.0 * squared)
    return (1.0 + radius) * jnp.exp(-radius)

def times_transposed(left_mat, right_mat):
    return lax.dot_general(left_mat.astype(jnp.float32), right_mat.astype(jnp.float32), (((1,), (1,)), ((), ())), precision=lax.Precision.HIGHEST, preferred_element_type=jnp.float32)

def lower_inverse(square):
    factor = jnp.linalg.cholesky(square)
    return jax.scipy.linalg.solve_triangular(factor, jnp.eye(square.shape[0], dtype=jnp.float32), lower=True)

def reference(left_factor, pick_site, noise):
    row_blocks, n_row, block_width, col_blocks, n_col, _ = left_factor.shape
    left_cols = col_blocks * n_col * block_width
    row_share = row_blocks * block_width // n_col
    head_rows = left_factor[0, :2].reshape(2 * block_width, left_cols)
    left_sums = jnp.einsum('arbk,sk->rabs', left_factor.reshape(row_blocks, n_row, block_width, left_cols), head_rows, precision=lax.Precision.HIGHEST)
    left_sums = left_sums.reshape(n_row * row_blocks * block_width, 2 * block_width)
    coords = site_coords(jnp.transpose(pick_site, (1, 0, 2)).reshape(-1))
    head_coords = site_coords(pick_site[0, :2].reshape(-1))
    noise_rows = jnp.transpose(noise, (1, 0, 2)).reshape(-1)
    second_start = row_blocks * block_width
    first_cov = matern(coords, head_coords[:, :block_width]) - left_sums[:, :block_width]
    first_cov = first_cov.at[:block_width].add(jnp.diag(noise_rows[:block_width]))
    first_panel = times_transposed(first_cov, lower_inverse(first_cov[:block_width]))
    cross_rows = first_panel[second_start:second_start + block_width]
    second_cov = matern(coords, head_coords[:, block_width:]) - left_sums[:, block_width:] - times_transposed(first_panel, cross_rows)
    second_cov = second_cov.at[second_start:second_start + block_width].add(jnp.diag(noise_rows[second_start:second_start + block_width]))
    second_panel = times_transposed(second_cov, lower_inverse(second_cov[second_start:second_start + block_width]))
    return jnp.stack([first_panel, second_panel], axis=1).reshape(n_row, n_col, row_share, 2, block_width)
```

```python
import jax
import jax.numpy as jnp
from jax import lax
from jax.sharding import PartitionSpec as P

GRID_Y = 64
GRID_Z = 32


LATERAL = 24.0
VERTICAL = 6.0


def site_coords(site_ids):
    coord_x = site_ids // (GRID_Y * GRID_Z)
    coord_y = site_ids // GRID_Z % GRID_Y
    coord_z = site_ids % GRID_Z
    return jnp.stack([coord_x, coord_y, coord_z]).astype(jnp.float32)


def matern(row_coords, col_coords):
    lengths = (LATERAL, LATERAL, VERTICAL)
    squared = jnp.zeros((row_coords.shape[1], col_coords.shape[1]), jnp.float32)
    for dim_index in range(3):
        difference = (row_coords[dim_index][:, None] - col_coords[dim_index][None, :]) / lengths[
            dim_index
        ]
        squared = squared + difference * difference
    radius = jnp.sqrt(3.0 * squared)
    return (1.0 + radius) * jnp.exp(-radius)


def times_transposed(left_mat, right_mat):
    return lax.dot_general(
        left_mat,
        right_mat,
        (((1,), (1,)), ((), ())),
        precision=lax.Precision.HIGHEST,
        preferred_element_type=jnp.float32,
    )


def lower_inverse(square):
    factor = jnp.linalg.cholesky(square)
    return jax.scipy.linalg.solve_triangular(
        factor, jnp.eye(square.shape[0], dtype=jnp.float32), lower=True
    )


def body(left_factor, pick_site, noise):
    row_blocks, _, block_width, col_blocks, _, _ = left_factor.shape
    col_count = lax.axis_size("col")
    row_share = row_blocks * block_width // col_count
    row_index = lax.axis_index("row")
    col_index = lax.axis_index("col")
    local_rows = left_factor.reshape(row_blocks * block_width, col_blocks * block_width)
    site_flat = pick_site.reshape(row_blocks * block_width)
    noise_flat = noise.reshape(row_blocks * block_width)
    offset = col_index * row_share
    my_coords = site_coords(lax.dynamic_slice_in_dim(site_flat, offset, row_share))
    my_noise = lax.dynamic_slice_in_dim(noise_flat, offset, row_share)
    first_owner = (row_index == 0) & (col_index == 0)
    second_owner = (row_index == 1) & (col_index == 0)
    own_diag = jnp.diag(my_noise[:block_width])

    head_rows = local_rows[:block_width]
    head_info = jnp.concatenate(
        [site_coords(site_flat[:block_width]), noise_flat[None, :block_width]], axis=0
    )
    is_first = row_index == 0
    is_second = row_index == 1
    heads = jnp.concatenate(
        [jnp.where(is_first, head_rows, 0.0), jnp.where(is_second, head_rows, 0.0)], axis=0
    )
    info = jnp.concatenate(
        [jnp.where(is_first, head_info, 0.0), jnp.where(is_second, head_info, 0.0)], axis=1
    )
    heads, info = lax.psum((heads, info), "row")

    terms = lax.dot_general(
        local_rows.reshape(col_count, row_share, col_blocks * block_width),
        heads,
        (((2,), (1,)), ((), ())),
        precision=lax.Precision.HIGHEST,
        preferred_element_type=jnp.float32,
    )
    gram = lax.psum(times_transposed(heads, heads), "col")
    sums = lax.psum_scatter(terms, "col", scatter_dimension=0, tiled=False)

    first_coords = info[:3, :block_width]
    second_coords = info[:3, block_width:]
    first_diag = matern(first_coords, first_coords) - gram[:block_width, :block_width]
    first_diag = first_diag + jnp.diag(info[3, :block_width])
    first_inverse = lower_inverse(first_diag)
    cross_rows = times_transposed(
        matern(second_coords, first_coords) - gram[block_width:, :block_width], first_inverse
    )
    second_diag = (
        matern(second_coords, second_coords)
        - gram[block_width:, block_width:]
        - times_transposed(cross_rows, cross_rows)
    )
    second_diag = second_diag + jnp.diag(info[3, block_width:])
    second_inverse = lower_inverse(second_diag)

    first_cov = matern(my_coords, first_coords) - sums[:, :block_width]
    first_cov = first_cov.at[:block_width].add(jnp.where(first_owner, own_diag, 0.0))
    first_panel = times_transposed(first_cov, first_inverse)
    second_cov = (
        (matern(my_coords, second_coords) - sums[:, block_width:])
        - times_transposed(first_panel, cross_rows)
    )
    second_cov = second_cov.at[:block_width].add(jnp.where(second_owner, own_diag, 0.0))
    second_panel = times_transposed(second_cov, second_inverse)
    stacked = jnp.stack([first_panel, second_panel], axis=1)
    return stacked.reshape(1, 1, row_share, 2, block_width)


def solution(mesh):
    placed = (P(None, "row", None, None, "col", None), P(None, "row", None), P(None, "row", None))
    return jax.shard_map(
        body,
        mesh=mesh,
        in_specs=placed,
        out_specs=P("row", "col", None, None, None),
        check_vma=False,
    )
```

```python
import jax
import jax.numpy as jnp
from jax import lax
from jax.sharding import PartitionSpec as P

GRID_Y = 64
GRID_Z = 32


LATERAL = 24.0
VERTICAL = 6.0


def site_coords(site_ids):
    coord_x = site_ids // (GRID_Y * GRID_Z)
    coord_y = site_ids // GRID_Z % GRID_Y
    coord_z = site_ids % GRID_Z
    return jnp.stack([coord_x, coord_y, coord_z]).astype(jnp.float32)


def matern(row_coords, col_coords):
    lengths = (LATERAL, LATERAL, VERTICAL)
    squared = jnp.zeros((row_coords.shape[1], col_coords.shape[1]), jnp.float32)
    for dim_index in range(3):
        difference = (row_coords[dim_index][:, None] - col_coords[dim_index][None, :]) / lengths[
            dim_index
        ]
        squared = squared + difference * difference
    radius = jnp.sqrt(3.0 * squared)
    return (1.0 + radius) * jnp.exp(-radius)


def times_transposed(left_mat, right_mat):
    return lax.dot_general(
        left_mat,
        right_mat,
        (((1,), (1,)), ((), ())),
        precision=lax.Precision.HIGHEST,
        preferred_element_type=jnp.float32,
    )


def lower_inverse(square):
    factor = jnp.linalg.cholesky(square)
    return jax.scipy.linalg.solve_triangular(
        factor, jnp.eye(square.shape[0], dtype=jnp.float32), lower=True
    )


def col_sum(block):
    count = lax.axis_size("col")
    step = 1
    while step < count:
        block = block + lax.ppermute(block, "col", [(i, i ^ step) for i in range(count)])
        step *= 2
    return block


def body(left_factor, pick_site, noise):
    row_blocks, _, block_width, col_blocks, _, _ = left_factor.shape
    col_count = lax.axis_size("col")
    row_share = row_blocks * block_width // col_count
    row_index = lax.axis_index("row")
    col_index = lax.axis_index("col")
    local_rows = left_factor.reshape(row_blocks * block_width, col_blocks * block_width)
    site_flat = pick_site.reshape(row_blocks * block_width)
    noise_flat = noise.reshape(row_blocks * block_width)
    offset = col_index * row_share
    my_coords = site_coords(lax.dynamic_slice_in_dim(site_flat, offset, row_share))
    my_noise = lax.dynamic_slice_in_dim(noise_flat, offset, row_share)
    first_owner = (row_index == 0) & (col_index == 0)
    second_owner = (row_index == 1) & (col_index == 0)
    own_diag = jnp.diag(my_noise[:block_width])

    head_rows = local_rows[:block_width]
    head_info = jnp.concatenate(
        [site_coords(site_flat[:block_width]), noise_flat[None, :block_width]], axis=0
    )
    is_first = row_index == 0
    is_second = row_index == 1
    heads = jnp.concatenate(
        [jnp.where(is_first, head_rows, 0.0), jnp.where(is_second, head_rows, 0.0)], axis=0
    )
    info = jnp.concatenate(
        [jnp.where(is_first, head_info, 0.0), jnp.where(is_second, head_info, 0.0)], axis=1
    )
    info_rows = jnp.zeros((8, heads.shape[1]), jnp.float32).at[:4, : 2 * block_width].set(info)
    packed = lax.psum(jnp.concatenate([heads, info_rows], axis=0), "row")
    heads = packed[: 2 * block_width]
    info = packed[2 * block_width : 2 * block_width + 4, : 2 * block_width]

    terms = times_transposed(local_rows, heads).reshape(col_count, row_share, 2 * block_width)
    sums = lax.psum_scatter(terms, "col", scatter_dimension=0, tiled=False)
    gram = col_sum(times_transposed(heads, heads))

    first_coords = info[:3, :block_width]
    second_coords = info[:3, block_width:]
    first_diag = matern(first_coords, first_coords) - gram[:block_width, :block_width]
    first_diag = first_diag + jnp.diag(info[3, :block_width])
    first_inverse = lower_inverse(first_diag)
    cross_rows = times_transposed(
        matern(second_coords, first_coords) - gram[block_width:, :block_width], first_inverse
    )
    second_diag = (
        matern(second_coords, second_coords)
        - gram[block_width:, block_width:]
        - times_transposed(cross_rows, cross_rows)
    )
    second_diag = second_diag + jnp.diag(info[3, block_width:])
    second_inverse = lower_inverse(second_diag)

    first_cov = matern(my_coords, first_coords) - sums[:, :block_width]
    first_cov = first_cov.at[:block_width].add(jnp.where(first_owner, own_diag, 0.0))
    first_panel = times_transposed(first_cov, first_inverse)
    second_cov = (
        (matern(my_coords, second_coords) - sums[:, block_width:])
        - times_transposed(first_panel, cross_rows)
    )
    second_cov = second_cov.at[:block_width].add(jnp.where(second_owner, own_diag, 0.0))
    second_panel = times_transposed(second_cov, second_inverse)
    stacked = jnp.stack([first_panel, second_panel], axis=1)
    return stacked.reshape(1, 1, row_share, 2, block_width)


def solution(mesh):
    placed = (P(None, "row", None, None, "col", None), P(None, "row", None), P(None, "row", None))
    return jax.shard_map(
        body,
        mesh=mesh,
        in_specs=placed,
        out_specs=P("row", "col", None, None, None),
        check_vma=False,
    )
```

```python
import jax
import jax.numpy as jnp
from jax import lax
from jax.sharding import PartitionSpec as P

GRID_Y = 64
GRID_Z = 32


LATERAL = 24.0
VERTICAL = 6.0


def site_coords(site_ids):
    coord_x = site_ids // (GRID_Y * GRID_Z)
    coord_y = site_ids // GRID_Z % GRID_Y
    coord_z = site_ids % GRID_Z
    return jnp.stack([coord_x, coord_y, coord_z]).astype(jnp.float32)


def matern(row_coords, col_coords):
    lengths = (LATERAL, LATERAL, VERTICAL)
    squared = jnp.zeros((row_coords.shape[1], col_coords.shape[1]), jnp.float32)
    for dim_index in range(3):
        difference = (row_coords[dim_index][:, None] - col_coords[dim_index][None, :]) / lengths[
            dim_index
        ]
        squared = squared + difference * difference
    radius = jnp.sqrt(3.0 * squared)
    return (1.0 + radius) * jnp.exp(-radius)


def times_transposed(left_mat, right_mat):
    return lax.dot_general(
        left_mat,
        right_mat,
        (((1,), (1,)), ((), ())),
        precision=lax.Precision.HIGHEST,
        preferred_element_type=jnp.float32,
    )


def lower_inverse(square):
    factor = jnp.linalg.cholesky(square)
    return jax.scipy.linalg.solve_triangular(
        factor, jnp.eye(square.shape[0], dtype=jnp.float32), lower=True
    )


def col_sum(block):
    count = lax.axis_size("col")
    step = 1
    while step < count:
        block = block + lax.ppermute(block, "col", [(i, i ^ step) for i in range(count)])
        step *= 2
    return block


def row_broadcast(pack):
    row = lax.axis_index("row")
    swap01 = lax.ppermute(pack, "row", [(0, 1), (1, 0)])
    to_next = lax.ppermute(pack, "row", [(0, 2), (1, 3)])
    to_prev = lax.ppermute(pack, "row", [(0, 6), (1, 7)])
    hand = jnp.where(row < 4, to_next, to_prev)
    swap_side = lax.ppermute(hand, "row", [(2, 3), (3, 2), (6, 7), (7, 6)])
    to_far = lax.ppermute(to_next, "row", [(2, 4), (3, 5)])
    swap_far = lax.ppermute(to_far, "row", [(4, 5), (5, 4)])
    chip = row // 2
    first_hand = jnp.where(
        chip == 0, pack, jnp.where(chip == 1, to_next, jnp.where(chip == 2, to_far, to_prev))
    )
    second_hand = jnp.where(chip == 0, swap01, jnp.where(chip == 2, swap_far, swap_side))
    return first_hand, second_hand


def col_scatter(blocks):
    count = lax.axis_size("col")
    me = lax.axis_index("col")
    bits = count.bit_length() - 1
    shaped = blocks.reshape((2,) * bits + blocks.shape[1:])
    remaining = list(range(bits - 1, -1, -1))
    for bit in (0, 2, 1, 3)[:bits] if bits == 4 else range(bits):
        axis = remaining.index(bit)
        mine = (me >> bit) % 2
        keep = lax.dynamic_index_in_dim(shaped, mine, axis, keepdims=False)
        send = lax.dynamic_index_in_dim(shaped, 1 - mine, axis, keepdims=False)
        shaped = keep + lax.ppermute(send, "col", [(i, i ^ (1 << bit)) for i in range(count)])
        remaining.pop(axis)
    return shaped


def body(left_factor, pick_site, noise):
    row_blocks, _, block_width, col_blocks, _, _ = left_factor.shape
    col_count = lax.axis_size("col")
    row_share = row_blocks * block_width // col_count
    row_index = lax.axis_index("row")
    col_index = lax.axis_index("col")
    local_rows = left_factor.reshape(row_blocks * block_width, col_blocks * block_width)
    site_flat = pick_site.reshape(row_blocks * block_width)
    noise_flat = noise.reshape(row_blocks * block_width)
    offset = col_index * row_share
    my_coords = site_coords(lax.dynamic_slice_in_dim(site_flat, offset, row_share))
    my_noise = lax.dynamic_slice_in_dim(noise_flat, offset, row_share)
    first_owner = (row_index == 0) & (col_index == 0)
    second_owner = (row_index == 1) & (col_index == 0)
    own_diag = jnp.diag(my_noise[:block_width])

    head_rows = local_rows[:block_width]
    head_info = jnp.concatenate(
        [site_coords(site_flat[:block_width]), noise_flat[None, :block_width]], axis=0
    )
    is_first = row_index == 0
    is_second = row_index == 1
    info_rows = jnp.zeros((8, head_rows.shape[1]), jnp.float32).at[:4, :block_width].set(head_info)
    first_hand, second_hand = row_broadcast(jnp.concatenate([head_rows, info_rows], axis=0))
    is_even = row_index % 2 == 0
    first_pack = jnp.where(is_even, first_hand, second_hand)
    second_pack = jnp.where(is_even, second_hand, first_hand)
    heads = jnp.concatenate([first_pack[:block_width], second_pack[:block_width]], axis=0)
    info = jnp.concatenate(
        [first_pack[block_width : block_width + 4, :block_width],
         second_pack[block_width : block_width + 4, :block_width]],
        axis=1,
    )

    gram = col_sum(times_transposed(heads, heads))
    terms = times_transposed(local_rows, heads).reshape(col_count, row_share, 2 * block_width)
    sums = col_scatter(terms)

    first_coords = info[:3, :block_width]
    second_coords = info[:3, block_width:]
    first_diag = matern(first_coords, first_coords) - gram[:block_width, :block_width]
    first_diag = first_diag + jnp.diag(info[3, :block_width])
    first_inverse = lower_inverse(first_diag)
    cross_rows = times_transposed(
        matern(second_coords, first_coords) - gram[block_width:, :block_width], first_inverse
    )
    second_diag = (
        matern(second_coords, second_coords)
        - gram[block_width:, block_width:]
        - times_transposed(cross_rows, cross_rows)
    )
    second_diag = second_diag + jnp.diag(info[3, block_width:])
    second_inverse = lower_inverse(second_diag)

    first_cov = matern(my_coords, first_coords) - sums[:, :block_width]
    first_cov = first_cov.at[:block_width].add(jnp.where(first_owner, own_diag, 0.0))
    first_panel = times_transposed(first_cov, first_inverse)
    second_cov = (
        (matern(my_coords, second_coords) - sums[:, block_width:])
        - times_transposed(first_panel, cross_rows)
    )
    second_cov = second_cov.at[:block_width].add(jnp.where(second_owner, own_diag, 0.0))
    second_panel = times_transposed(second_cov, second_inverse)
    stacked = jnp.stack([first_panel, second_panel], axis=1)
    return stacked.reshape(1, 1, row_share, 2, block_width)


def solution(mesh):
    placed = (P(None, "row", None, None, "col", None), P(None, "row", None), P(None, "row", None))
    return jax.shard_map(
        body,
        mesh=mesh,
        in_specs=placed,
        out_specs=P("row", "col", None, None, None),
        check_vma=False,
    )
```

```python
import jax
import jax.numpy as jnp
from jax import lax
from jax.sharding import PartitionSpec as P

GRID_Y = 64
GRID_Z = 32


LATERAL = 24.0
VERTICAL = 6.0


def site_coords(site_ids):
    coord_x = site_ids // (GRID_Y * GRID_Z)
    coord_y = site_ids // GRID_Z % GRID_Y
    coord_z = site_ids % GRID_Z
    return jnp.stack([coord_x, coord_y, coord_z]).astype(jnp.float32)


def matern(row_coords, col_coords):
    lengths = (LATERAL, LATERAL, VERTICAL)
    squared = jnp.zeros((row_coords.shape[1], col_coords.shape[1]), jnp.float32)
    for dim_index in range(3):
        difference = (row_coords[dim_index][:, None] - col_coords[dim_index][None, :]) / lengths[
            dim_index
        ]
        squared = squared + difference * difference
    radius = jnp.sqrt(3.0 * squared)
    return (1.0 + radius) * jnp.exp(-radius)


def times_transposed(left_mat, right_mat):
    return lax.dot_general(
        left_mat,
        right_mat,
        (((1,), (1,)), ((), ())),
        precision=lax.Precision.HIGHEST,
        preferred_element_type=jnp.float32,
    )


def lower_inverse(square):
    factor = jnp.linalg.cholesky(square)
    return jax.scipy.linalg.solve_triangular(
        factor, jnp.eye(square.shape[0], dtype=jnp.float32), lower=True
    )


def col_sum(block):
    count = lax.axis_size("col")
    group = 1
    while group < count:
        width = min(4, count // group)
        parts = [
            lax.ppermute(block, "col", [(i, i ^ (k * group)) for i in range(count)])
            for k in range(1, width)
        ]
        for part in parts:
            block = block + part
        group *= width
    return block


def row_broadcast(pack):
    row = lax.axis_index("row")
    swap_home = lax.ppermute(pack, "row", [(0, 1), (1, 0)])
    first_out = lax.ppermute(pack, "row", [(0, 2), (1, 7)])
    relay = lax.ppermute(first_out, "row", [(2, 4), (7, 5)])
    second_out = lax.ppermute(
        jnp.where(row < 2, pack, first_out), "row", [(1, 3), (0, 6)]
    )
    hand = jnp.where(
        row < 2,
        pack,
        jnp.where((row == 2) | (row == 7), first_out, jnp.where((row == 4) | (row == 5), relay, second_out)),
    )
    swap_far = lax.ppermute(hand, "row", [(2, 3), (3, 2), (4, 5), (5, 4), (6, 7), (7, 6)])
    other = jnp.where(row < 2, swap_home, swap_far)
    return hand, other


def col_scatter(blocks):
    count = lax.axis_size("col")
    me = lax.axis_index("col")
    bits = count.bit_length() - 1
    shaped = blocks.reshape((2,) * bits + blocks.shape[1:])
    remaining = list(range(bits - 1, -1, -1))
    for bit in (0, 2, 1, 3)[:bits] if bits == 4 else range(bits):
        axis = remaining.index(bit)
        mine = (me >> bit) % 2
        keep = lax.dynamic_index_in_dim(shaped, mine, axis, keepdims=False)
        send = lax.dynamic_index_in_dim(shaped, 1 - mine, axis, keepdims=False)
        shaped = keep + lax.ppermute(send, "col", [(i, i ^ (1 << bit)) for i in range(count)])
        remaining.pop(axis)
    return shaped


def body(left_factor, pick_site, noise):
    row_blocks, _, block_width, col_blocks, _, _ = left_factor.shape
    col_count = lax.axis_size("col")
    row_share = row_blocks * block_width // col_count
    row_index = lax.axis_index("row")
    col_index = lax.axis_index("col")
    local_rows = left_factor.reshape(row_blocks * block_width, col_blocks * block_width)
    site_flat = pick_site.reshape(row_blocks * block_width)
    noise_flat = noise.reshape(row_blocks * block_width)
    offset = col_index * row_share
    my_coords = site_coords(lax.dynamic_slice_in_dim(site_flat, offset, row_share))
    my_noise = lax.dynamic_slice_in_dim(noise_flat, offset, row_share)
    first_owner = (row_index == 0) & (col_index == 0)
    second_owner = (row_index == 1) & (col_index == 0)
    own_diag = jnp.diag(my_noise[:block_width])

    head_rows = local_rows[:block_width]
    head_info = jnp.concatenate(
        [site_coords(site_flat[:block_width]), noise_flat[None, :block_width]], axis=0
    )
    is_first = row_index == 0
    is_second = row_index == 1
    info_rows = jnp.zeros((8, head_rows.shape[1]), jnp.float32).at[:4, :block_width].set(head_info)
    hand, other = row_broadcast(jnp.concatenate([head_rows, info_rows], axis=0))
    is_even = row_index % 2 == 0
    first_pack = jnp.where(is_even, hand, other)
    second_pack = jnp.where(is_even, other, hand)
    heads = jnp.concatenate([first_pack[:block_width], second_pack[:block_width]], axis=0)
    info = jnp.concatenate(
        [first_pack[block_width : block_width + 4, :block_width],
         second_pack[block_width : block_width + 4, :block_width]],
        axis=1,
    )

    gram = col_sum(times_transposed(heads, heads))
    terms = times_transposed(local_rows, heads).reshape(col_count, row_share, 2 * block_width)
    sums = col_scatter(terms)

    first_coords = info[:3, :block_width]
    second_coords = info[:3, block_width:]
    first_diag = matern(first_coords, first_coords) - gram[:block_width, :block_width]
    first_diag = first_diag + jnp.diag(info[3, :block_width])
    first_inverse = lower_inverse(first_diag)
    cross_rows = times_transposed(
        matern(second_coords, first_coords) - gram[block_width:, :block_width], first_inverse
    )
    second_diag = (
        matern(second_coords, second_coords)
        - gram[block_width:, block_width:]
        - times_transposed(cross_rows, cross_rows)
    )
    second_diag = second_diag + jnp.diag(info[3, block_width:])
    second_inverse = lower_inverse(second_diag)

    first_cov = matern(my_coords, first_coords) - sums[:, :block_width]
    first_cov = first_cov.at[:block_width].add(jnp.where(first_owner, own_diag, 0.0))
    first_panel = times_transposed(first_cov, first_inverse)
    second_cov = (
        (matern(my_coords, second_coords) - sums[:, block_width:])
        - times_transposed(first_panel, cross_rows)
    )
    second_cov = second_cov.at[:block_width].add(jnp.where(second_owner, own_diag, 0.0))
    second_panel = times_transposed(second_cov, second_inverse)
    stacked = jnp.stack([first_panel, second_panel], axis=1)
    return stacked.reshape(1, 1, row_share, 2, block_width)


def solution(mesh):
    placed = (P(None, "row", None, None, "col", None), P(None, "row", None), P(None, "row", None))
    return jax.shard_map(
        body,
        mesh=mesh,
        in_specs=placed,
        out_specs=P("row", "col", None, None, None),
        check_vma=False,
    )
```

```python
import jax
import jax.numpy as jnp
from jax import lax
from jax.sharding import PartitionSpec as P

GRID_Y = 64
GRID_Z = 32


LATERAL = 24.0
VERTICAL = 6.0


def site_coords(site_ids):
    coord_x = site_ids // (GRID_Y * GRID_Z)
    coord_y = site_ids // GRID_Z % GRID_Y
    coord_z = site_ids % GRID_Z
    return jnp.stack([coord_x, coord_y, coord_z]).astype(jnp.float32)


def matern(row_coords, col_coords):
    lengths = (LATERAL, LATERAL, VERTICAL)
    squared = jnp.zeros((row_coords.shape[1], col_coords.shape[1]), jnp.float32)
    for dim_index in range(3):
        difference = (row_coords[dim_index][:, None] - col_coords[dim_index][None, :]) / lengths[
            dim_index
        ]
        squared = squared + difference * difference
    radius = jnp.sqrt(3.0 * squared)
    return (1.0 + radius) * jnp.exp(-radius)


def times_transposed(left_mat, right_mat, precision=lax.Precision.HIGHEST):
    return lax.dot_general(
        left_mat,
        right_mat,
        (((1,), (1,)), ((), ())),
        precision=precision,
        preferred_element_type=jnp.float32,
    )


def lower_inverse(square):
    factor = jnp.linalg.cholesky(square)
    return jax.scipy.linalg.solve_triangular(
        factor, jnp.eye(square.shape[0], dtype=jnp.float32), lower=True
    )


def col_sum(block):
    count = lax.axis_size("col")
    group = 1
    while group < count:
        width = min(4, count // group)
        parts = [
            lax.ppermute(block, "col", [(i, i ^ (k * group)) for i in range(count)])
            for k in range(1, width)
        ]
        for part in parts:
            block = block + part
        group *= width
    return block


def row_broadcast(pack):
    row = lax.axis_index("row")
    swap_home = lax.ppermute(pack, "row", [(0, 1), (1, 0)])
    first_out = lax.ppermute(pack, "row", [(0, 2), (1, 7)])
    relay = lax.ppermute(first_out, "row", [(2, 4), (7, 5)])
    second_out = lax.ppermute(
        jnp.where(row < 2, pack, first_out), "row", [(1, 3), (0, 6)]
    )
    hand = jnp.where(
        row < 2,
        pack,
        jnp.where((row == 2) | (row == 7), first_out, jnp.where((row == 4) | (row == 5), relay, second_out)),
    )
    swap_far = lax.ppermute(hand, "row", [(2, 3), (3, 2), (4, 5), (5, 4), (6, 7), (7, 6)])
    other = jnp.where(row < 2, swap_home, swap_far)
    return hand, other


def col_scatter(blocks):
    count = lax.axis_size("col")
    me = lax.axis_index("col")
    bits = count.bit_length() - 1
    shaped = blocks.reshape((2,) * bits + blocks.shape[1:])
    remaining = list(range(bits - 1, -1, -1))
    for bit in (0, 2, 1, 3)[:bits] if bits == 4 else range(bits):
        axis = remaining.index(bit)
        mine = (me >> bit) % 2
        keep = lax.dynamic_index_in_dim(shaped, mine, axis, keepdims=False)
        send = lax.dynamic_index_in_dim(shaped, 1 - mine, axis, keepdims=False)
        shaped = keep + lax.ppermute(send, "col", [(i, i ^ (1 << bit)) for i in range(count)])
        remaining.pop(axis)
    return shaped


def body(left_factor, pick_site, noise):
    row_blocks, _, block_width, col_blocks, _, _ = left_factor.shape
    col_count = lax.axis_size("col")
    row_share = row_blocks * block_width // col_count
    row_index = lax.axis_index("row")
    col_index = lax.axis_index("col")
    local_rows = left_factor.reshape(row_blocks * block_width, col_blocks * block_width)
    site_flat = pick_site.reshape(row_blocks * block_width)
    noise_flat = noise.reshape(row_blocks * block_width)
    offset = col_index * row_share
    my_coords = site_coords(lax.dynamic_slice_in_dim(site_flat, offset, row_share))
    my_noise = lax.dynamic_slice_in_dim(noise_flat, offset, row_share)
    first_owner = (row_index == 0) & (col_index == 0)
    second_owner = (row_index == 1) & (col_index == 0)
    own_diag = jnp.diag(my_noise[:block_width])

    head_rows = local_rows[:block_width]
    head_info = jnp.concatenate(
        [site_coords(site_flat[:block_width]), noise_flat[None, :block_width]], axis=0
    )
    is_first = row_index == 0
    is_second = row_index == 1
    info_rows = jnp.zeros((8, head_rows.shape[1]), jnp.float32).at[:4, :block_width].set(head_info)
    hand, other = row_broadcast(jnp.concatenate([head_rows, info_rows], axis=0))
    is_even = row_index % 2 == 0
    first_pack = jnp.where(is_even, hand, other)
    second_pack = jnp.where(is_even, other, hand)
    heads = jnp.concatenate([first_pack[:block_width], second_pack[:block_width]], axis=0)
    info = jnp.concatenate(
        [first_pack[block_width : block_width + 4, :block_width],
         second_pack[block_width : block_width + 4, :block_width]],
        axis=1,
    )

    gram = col_sum(times_transposed(heads, heads))
    terms = times_transposed(local_rows, heads, lax.Precision.HIGH).reshape(
        col_count, row_share, 2 * block_width
    )
    sums = col_scatter(terms)

    first_coords = info[:3, :block_width]
    second_coords = info[:3, block_width:]
    first_diag = matern(first_coords, first_coords) - gram[:block_width, :block_width]
    first_diag = first_diag + jnp.diag(info[3, :block_width])
    first_inverse = lower_inverse(first_diag)
    cross_rows = times_transposed(
        matern(second_coords, first_coords) - gram[block_width:, :block_width], first_inverse
    )
    second_diag = (
        matern(second_coords, second_coords)
        - gram[block_width:, block_width:]
        - times_transposed(cross_rows, cross_rows)
    )
    second_diag = second_diag + jnp.diag(info[3, block_width:])
    second_inverse = lower_inverse(second_diag)

    first_cov = matern(my_coords, first_coords) - sums[:, :block_width]
    first_cov = first_cov.at[:block_width].add(jnp.where(first_owner, own_diag, 0.0))
    first_panel = times_transposed(first_cov, first_inverse)
    second_cov = (
        (matern(my_coords, second_coords) - sums[:, block_width:])
        - times_transposed(first_panel, cross_rows)
    )
    second_cov = second_cov.at[:block_width].add(jnp.where(second_owner, own_diag, 0.0))
    second_panel = times_transposed(second_cov, second_inverse)
    stacked = jnp.stack([first_panel, second_panel], axis=1)
    return stacked.reshape(1, 1, row_share, 2, block_width)


def solution(mesh):
    placed = (P(None, "row", None, None, "col", None), P(None, "row", None), P(None, "row", None))
    return jax.shard_map(
        body,
        mesh=mesh,
        in_specs=placed,
        out_specs=P("row", "col", None, None, None),
        check_vma=False,
    )
```

```python
import jax
import jax.numpy as jnp
from jax import lax
from jax.sharding import PartitionSpec as P

GRID_Y = 64
GRID_Z = 32


LATERAL = 24.0
VERTICAL = 6.0


def site_coords(site_ids):
    coord_x = site_ids // (GRID_Y * GRID_Z)
    coord_y = site_ids // GRID_Z % GRID_Y
    coord_z = site_ids % GRID_Z
    return jnp.stack([coord_x, coord_y, coord_z]).astype(jnp.float32)


def matern(row_coords, col_coords):
    lengths = (LATERAL, LATERAL, VERTICAL)
    squared = jnp.zeros((row_coords.shape[1], col_coords.shape[1]), jnp.float32)
    for dim_index in range(3):
        difference = (row_coords[dim_index][:, None] - col_coords[dim_index][None, :]) / lengths[
            dim_index
        ]
        squared = squared + difference * difference
    radius = jnp.sqrt(3.0 * squared)
    return (1.0 + radius) * jnp.exp(-radius)


def times_transposed(left_mat, right_mat, precision=lax.Precision.HIGHEST):
    return lax.dot_general(
        left_mat,
        right_mat,
        (((1,), (1,)), ((), ())),
        precision=precision,
        preferred_element_type=jnp.float32,
    )


def lower_inverse(square):
    factor = jnp.linalg.cholesky(square)
    half = square.shape[0] // 2
    corners = jnp.stack([factor[:half, :half], factor[half:, half:]])
    unit = jnp.broadcast_to(jnp.eye(half, dtype=jnp.float32), corners.shape)
    inverses = jax.scipy.linalg.solve_triangular(corners, unit, lower=True)
    upper_inv, lower_inv = inverses[0], inverses[1]
    below = -lax.dot(
        lax.dot(lower_inv, factor[half:, :half], precision=lax.Precision.HIGHEST),
        upper_inv,
        precision=lax.Precision.HIGHEST,
    )
    top = jnp.concatenate([upper_inv, jnp.zeros_like(upper_inv)], axis=1)
    return jnp.concatenate([top, jnp.concatenate([below, lower_inv], axis=1)], axis=0)


def col_sum(block):
    count = lax.axis_size("col")
    group = 1
    while group < count:
        width = min(4, count // group)
        parts = [
            lax.ppermute(block, "col", [(i, i ^ (k * group)) for i in range(count)])
            for k in range(1, width)
        ]
        for part in parts:
            block = block + part
        group *= width
    return block


def row_broadcast(pack):
    row = lax.axis_index("row")

    def send(value, pairs):
        cut = value.shape[0] // 2
        return jnp.concatenate(
            [lax.ppermute(value[:cut], "row", pairs), lax.ppermute(value[cut:], "row", pairs)], axis=0
        )

    swap_home = send(pack, [(0, 1), (1, 0)])
    first_out = send(pack, [(0, 2), (1, 7)])
    relay = send(first_out, [(2, 4), (7, 5)])
    second_out = send(
        jnp.where(row < 2, pack, first_out), [(1, 3), (0, 6)]
    )
    hand = jnp.where(
        row < 2,
        pack,
        jnp.where((row == 2) | (row == 7), first_out, jnp.where((row == 4) | (row == 5), relay, second_out)),
    )
    swap_far = send(hand, [(2, 3), (3, 2), (4, 5), (5, 4), (6, 7), (7, 6)])
    other = jnp.where(row < 2, swap_home, swap_far)
    return hand, other


def col_scatter(blocks):
    count = lax.axis_size("col")
    me = lax.axis_index("col")
    bits = count.bit_length() - 1
    shaped = blocks.reshape((2,) * bits + blocks.shape[1:])
    remaining = list(range(bits - 1, -1, -1))
    for bit in (0, 2, 1, 3)[:bits] if bits == 4 else range(bits):
        axis = remaining.index(bit)
        mine = (me >> bit) % 2
        keep = lax.dynamic_index_in_dim(shaped, mine, axis, keepdims=False)
        send = lax.dynamic_index_in_dim(shaped, 1 - mine, axis, keepdims=False)
        shaped = keep + lax.ppermute(send, "col", [(i, i ^ (1 << bit)) for i in range(count)])
        remaining.pop(axis)
    return shaped


def body(left_factor, pick_site, noise):
    row_blocks, _, block_width, col_blocks, _, _ = left_factor.shape
    col_count = lax.axis_size("col")
    row_share = row_blocks * block_width // col_count
    row_index = lax.axis_index("row")
    col_index = lax.axis_index("col")
    local_rows = left_factor.reshape(row_blocks * block_width, col_blocks * block_width)
    site_flat = pick_site.reshape(row_blocks * block_width)
    noise_flat = noise.reshape(row_blocks * block_width)
    offset = col_index * row_share
    my_coords = site_coords(lax.dynamic_slice_in_dim(site_flat, offset, row_share))
    my_noise = lax.dynamic_slice_in_dim(noise_flat, offset, row_share)
    first_owner = (row_index == 0) & (col_index == 0)
    second_owner = (row_index == 1) & (col_index == 0)
    own_diag = jnp.diag(my_noise[:block_width])

    head_rows = local_rows[:block_width]
    head_info = jnp.concatenate(
        [site_coords(site_flat[:block_width]), noise_flat[None, :block_width]], axis=0
    )
    is_first = row_index == 0
    is_second = row_index == 1
    info_rows = jnp.zeros((8, head_rows.shape[1]), jnp.float32).at[:4, :block_width].set(head_info)
    hand, other = row_broadcast(jnp.concatenate([head_rows, info_rows], axis=0))
    is_even = row_index % 2 == 0
    first_pack = jnp.where(is_even, hand, other)
    second_pack = jnp.where(is_even, other, hand)
    heads = jnp.concatenate([first_pack[:block_width], second_pack[:block_width]], axis=0)
    info = jnp.concatenate(
        [first_pack[block_width : block_width + 4, :block_width],
         second_pack[block_width : block_width + 4, :block_width]],
        axis=1,
    )

    gram_blocks = col_sum(
        jnp.concatenate(
            [times_transposed(heads, heads[:block_width]),
             times_transposed(heads[block_width:], heads[block_width:])],
            axis=0,
        )
    )
    gram_11 = gram_blocks[:block_width]
    gram_21 = gram_blocks[block_width : 2 * block_width]
    gram_22 = gram_blocks[2 * block_width :]
    terms = times_transposed(local_rows, heads, lax.Precision.HIGH).reshape(
        col_count, row_share, 2 * block_width
    )
    sums = col_scatter(terms)

    first_coords = info[:3, :block_width]
    second_coords = info[:3, block_width:]
    first_diag = matern(first_coords, first_coords) - gram_11
    first_diag = first_diag + jnp.diag(info[3, :block_width])
    first_inverse = lower_inverse(first_diag)
    cross_rows = times_transposed(
        matern(second_coords, first_coords) - gram_21, first_inverse
    )
    second_diag = (
        matern(second_coords, second_coords)
        - gram_22
        - times_transposed(cross_rows, cross_rows)
    )
    second_diag = second_diag + jnp.diag(info[3, block_width:])
    second_inverse = lower_inverse(second_diag)

    first_cov = matern(my_coords, first_coords) - sums[:, :block_width]
    first_cov = first_cov.at[:block_width].add(jnp.where(first_owner, own_diag, 0.0))
    first_panel = times_transposed(first_cov, first_inverse)
    second_cov = (
        (matern(my_coords, second_coords) - sums[:, block_width:])
        - times_transposed(first_panel, cross_rows)
    )
    second_cov = second_cov.at[:block_width].add(jnp.where(second_owner, own_diag, 0.0))
    second_panel = times_transposed(second_cov, second_inverse)
    stacked = jnp.stack([first_panel, second_panel], axis=1)
    return stacked.reshape(1, 1, row_share, 2, block_width)


def solution(mesh):
    placed = (P(None, "row", None, None, "col", None), P(None, "row", None), P(None, "row", None))
    return jax.shard_map(
        body,
        mesh=mesh,
        in_specs=placed,
        out_specs=P("row", "col", None, None, None),
        check_vma=False,
    )
```

```python
import jax
import jax.numpy as jnp
from jax import lax
from jax.sharding import PartitionSpec as P

GRID_Y = 64
GRID_Z = 32


LATERAL = 24.0
VERTICAL = 6.0


def site_coords(site_ids):
    coord_x = site_ids // (GRID_Y * GRID_Z)
    coord_y = site_ids // GRID_Z % GRID_Y
    coord_z = site_ids % GRID_Z
    return jnp.stack([coord_x, coord_y, coord_z]).astype(jnp.float32)


def matern(row_coords, col_coords):
    lengths = (LATERAL, LATERAL, VERTICAL)
    squared = jnp.zeros((row_coords.shape[1], col_coords.shape[1]), jnp.float32)
    for dim_index in range(3):
        difference = (row_coords[dim_index][:, None] - col_coords[dim_index][None, :]) / lengths[
            dim_index
        ]
        squared = squared + difference * difference
    radius = jnp.sqrt(3.0 * squared)
    return (1.0 + radius) * jnp.exp(-radius)


def times_transposed(left_mat, right_mat, precision=lax.Precision.HIGHEST):
    return lax.dot_general(
        left_mat,
        right_mat,
        (((1,), (1,)), ((), ())),
        precision=precision,
        preferred_element_type=jnp.float32,
    )


def lower_inverse(square):
    factor = jnp.linalg.cholesky(square)
    return jax.scipy.linalg.solve_triangular(
        factor, jnp.eye(square.shape[0], dtype=jnp.float32), lower=True
    )


def col_sum(block):
    count = lax.axis_size("col")
    group = 1
    while group < count:
        width = min(4, count // group)
        parts = [
            lax.ppermute(block, "col", [(i, i ^ (k * group)) for i in range(count)])
            for k in range(1, width)
        ]
        for part in parts:
            block = block + part
        group *= width
    return block


def row_broadcast(pack):
    row = lax.axis_index("row")
    swap_home = lax.ppermute(pack, "row", [(0, 1), (1, 0)])
    first_out = lax.ppermute(pack, "row", [(0, 2), (1, 7)])
    relay = lax.ppermute(first_out, "row", [(2, 4), (7, 5)])
    second_out = lax.ppermute(
        jnp.where(row < 2, pack, first_out), "row", [(1, 3), (0, 6)]
    )
    hand = jnp.where(
        row < 2,
        pack,
        jnp.where((row == 2) | (row == 7), first_out, jnp.where((row == 4) | (row == 5), relay, second_out)),
    )
    swap_far = lax.ppermute(hand, "row", [(2, 3), (3, 2), (4, 5), (5, 4), (6, 7), (7, 6)])
    other = jnp.where(row < 2, swap_home, swap_far)
    return hand, other, swap_home


def home_gram(block, count):
    def pairs(shift):
        return [(r * count + c, r * count + (c ^ shift)) for r in (0, 1) for c in range(count)]

    group = 1
    while group < count:
        width = min(4, count // group)
        parts = [lax.ppermute(block, ("row", "col"), pairs(k * group)) for k in range(1, width)]
        for part in parts:
            block = block + part
        group *= width
    row = lax.axis_index("row")
    near = lax.ppermute(block, "row", [(0, 2), (1, 7)])
    back = lax.ppermute(block, "row", [(0, 6), (1, 3)])
    far = lax.ppermute(near, "row", [(2, 4), (7, 5)])
    return jnp.where(
        row < 2,
        block,
        jnp.where((row == 2) | (row == 7), near, jnp.where((row == 3) | (row == 6), back, far)),
    )


def col_scatter(blocks):
    count = lax.axis_size("col")
    me = lax.axis_index("col")
    bits = count.bit_length() - 1
    shaped = blocks.reshape((2,) * bits + blocks.shape[1:])
    remaining = list(range(bits - 1, -1, -1))
    for bit in (0, 2, 1, 3)[:bits] if bits == 4 else range(bits):
        axis = remaining.index(bit)
        mine = (me >> bit) % 2
        keep = lax.dynamic_index_in_dim(shaped, mine, axis, keepdims=False)
        send = lax.dynamic_index_in_dim(shaped, 1 - mine, axis, keepdims=False)
        shaped = keep + lax.ppermute(send, "col", [(i, i ^ (1 << bit)) for i in range(count)])
        remaining.pop(axis)
    return shaped


def body(left_factor, pick_site, noise):
    row_blocks, _, block_width, col_blocks, _, _ = left_factor.shape
    col_count = lax.axis_size("col")
    row_share = row_blocks * block_width // col_count
    row_index = lax.axis_index("row")
    col_index = lax.axis_index("col")
    local_rows = left_factor.reshape(row_blocks * block_width, col_blocks * block_width)
    site_flat = pick_site.reshape(row_blocks * block_width)
    noise_flat = noise.reshape(row_blocks * block_width)
    offset = col_index * row_share
    my_coords = site_coords(lax.dynamic_slice_in_dim(site_flat, offset, row_share))
    my_noise = lax.dynamic_slice_in_dim(noise_flat, offset, row_share)
    first_owner = (row_index == 0) & (col_index == 0)
    second_owner = (row_index == 1) & (col_index == 0)
    own_diag = jnp.diag(my_noise[:block_width])

    head_rows = local_rows[:block_width]
    head_info = jnp.concatenate(
        [site_coords(site_flat[:block_width]), noise_flat[None, :block_width]], axis=0
    )
    is_first = row_index == 0
    is_second = row_index == 1
    info_rows = jnp.zeros((8, head_rows.shape[1]), jnp.float32).at[:4, :block_width].set(head_info)
    hand, other, swap_home = row_broadcast(jnp.concatenate([head_rows, info_rows], axis=0))
    is_even = row_index % 2 == 0
    first_pack = jnp.where(is_even, hand, other)
    second_pack = jnp.where(is_even, other, hand)
    heads = jnp.concatenate([first_pack[:block_width], second_pack[:block_width]], axis=0)
    info = jnp.concatenate(
        [first_pack[block_width : block_width + 4, :block_width],
         second_pack[block_width : block_width + 4, :block_width]],
        axis=1,
    )

    home_pack = jnp.concatenate(
        [jnp.where(is_even, head_rows, swap_home[:block_width]),
         jnp.where(is_even, swap_home[:block_width], head_rows)],
        axis=0,
    )
    gram = home_gram(times_transposed(home_pack, home_pack), col_count)
    terms = times_transposed(local_rows, heads, lax.Precision.HIGH).reshape(
        col_count, row_share, 2 * block_width
    )
    sums = col_scatter(terms)

    first_coords = info[:3, :block_width]
    second_coords = info[:3, block_width:]
    first_diag = matern(first_coords, first_coords) - gram[:block_width, :block_width]
    first_diag = first_diag + jnp.diag(info[3, :block_width])
    first_inverse = lower_inverse(first_diag)
    cross_rows = times_transposed(
        matern(second_coords, first_coords) - gram[block_width:, :block_width], first_inverse
    )
    second_diag = (
        matern(second_coords, second_coords)
        - gram[block_width:, block_width:]
        - times_transposed(cross_rows, cross_rows)
    )
    second_diag = second_diag + jnp.diag(info[3, block_width:])
    second_inverse = lower_inverse(second_diag)

    first_cov = matern(my_coords, first_coords) - sums[:, :block_width]
    first_cov = first_cov.at[:block_width].add(jnp.where(first_owner, own_diag, 0.0))
    first_panel = times_transposed(first_cov, first_inverse)
    second_cov = (
        (matern(my_coords, second_coords) - sums[:, block_width:])
        - times_transposed(first_panel, cross_rows)
    )
    second_cov = second_cov.at[:block_width].add(jnp.where(second_owner, own_diag, 0.0))
    second_panel = times_transposed(second_cov, second_inverse)
    stacked = jnp.stack([first_panel, second_panel], axis=1)
    return stacked.reshape(1, 1, row_share, 2, block_width)


def solution(mesh):
    placed = (P(None, "row", None, None, "col", None), P(None, "row", None), P(None, "row", None))
    return jax.shard_map(
        body,
        mesh=mesh,
        in_specs=placed,
        out_specs=P("row", "col", None, None, None),
        check_vma=False,
    )
```

```python
import jax
import jax.numpy as jnp
from jax import lax
from jax.sharding import PartitionSpec as P

GRID_Y = 64
GRID_Z = 32


LATERAL = 24.0
VERTICAL = 6.0


def site_coords(site_ids):
    coord_x = site_ids // (GRID_Y * GRID_Z)
    coord_y = site_ids // GRID_Z % GRID_Y
    coord_z = site_ids % GRID_Z
    return jnp.stack([coord_x, coord_y, coord_z]).astype(jnp.float32)


def matern(row_coords, col_coords):
    lengths = (LATERAL, LATERAL, VERTICAL)
    squared = jnp.zeros((row_coords.shape[1], col_coords.shape[1]), jnp.float32)
    for dim_index in range(3):
        difference = (row_coords[dim_index][:, None] - col_coords[dim_index][None, :]) / lengths[
            dim_index
        ]
        squared = squared + difference * difference
    radius = jnp.sqrt(3.0 * squared)
    return (1.0 + radius) * jnp.exp(-radius)


def times_transposed(left_mat, right_mat, precision=lax.Precision.HIGHEST):
    return lax.dot_general(
        left_mat,
        right_mat,
        (((1,), (1,)), ((), ())),
        precision=precision,
        preferred_element_type=jnp.float32,
    )


def lower_inverse(square):
    factor = jnp.linalg.cholesky(square)
    return jax.scipy.linalg.solve_triangular(
        factor, jnp.eye(square.shape[0], dtype=jnp.float32), lower=True
    )


def col_sum(block):
    count = lax.axis_size("col")
    group = 1
    while group < count:
        width = min(4, count // group)
        parts = [
            lax.ppermute(block, "col", [(i, i ^ (k * group)) for i in range(count)])
            for k in range(1, width)
        ]
        for part in parts:
            block = block + part
        group *= width
    return block


def row_broadcast(pack):
    row = lax.axis_index("row")
    swap_home = lax.ppermute(pack, "row", [(0, 1), (1, 0)])
    first_out = lax.ppermute(pack, "row", [(0, 2), (1, 7)])
    relay = lax.ppermute(first_out, "row", [(2, 4), (7, 5)])
    second_out = lax.ppermute(
        jnp.where(row < 2, pack, first_out), "row", [(1, 3), (0, 6)]
    )
    hand = jnp.where(
        row < 2,
        pack,
        jnp.where((row == 2) | (row == 7), first_out, jnp.where((row == 4) | (row == 5), relay, second_out)),
    )
    swap_far = lax.ppermute(hand, "row", [(2, 3), (3, 2), (4, 5), (5, 4), (6, 7), (7, 6)])
    other = jnp.where(row < 2, swap_home, swap_far)
    return hand, other


def col_scatter(blocks):
    count = lax.axis_size("col")
    me = lax.axis_index("col")
    bits = count.bit_length() - 1
    shaped = blocks.reshape((2,) * bits + blocks.shape[1:])
    remaining = list(range(bits - 1, -1, -1))
    for bit in (0, 2, 1, 3)[:bits] if bits == 4 else range(bits):
        axis = remaining.index(bit)
        mine = (me >> bit) % 2
        keep = lax.dynamic_index_in_dim(shaped, mine, axis, keepdims=False)
        send = lax.dynamic_index_in_dim(shaped, 1 - mine, axis, keepdims=False)
        shaped = keep + lax.ppermute(send, "col", [(i, i ^ (1 << bit)) for i in range(count)])
        remaining.pop(axis)
    return shaped


def body(left_factor, pick_site, noise):
    row_blocks, _, block_width, col_blocks, _, _ = left_factor.shape
    col_count = lax.axis_size("col")
    row_share = row_blocks * block_width // col_count
    row_index = lax.axis_index("row")
    col_index = lax.axis_index("col")
    local_rows = left_factor.reshape(row_blocks * block_width, col_blocks * block_width)
    site_flat = pick_site.reshape(row_blocks * block_width)
    noise_flat = noise.reshape(row_blocks * block_width)
    offset = col_index * row_share
    my_coords = site_coords(lax.dynamic_slice_in_dim(site_flat, offset, row_share))
    my_noise = lax.dynamic_slice_in_dim(noise_flat, offset, row_share)
    first_owner = (row_index == 0) & (col_index == 0)
    second_owner = (row_index == 1) & (col_index == 0)
    own_diag = jnp.diag(my_noise[:block_width])

    head_rows = local_rows[:block_width]
    head_info = jnp.concatenate(
        [site_coords(site_flat[:block_width]), noise_flat[None, :block_width]], axis=0
    )
    is_first = row_index == 0
    is_second = row_index == 1
    info_rows = jnp.zeros((8, head_rows.shape[1]), jnp.float32).at[:4, :block_width].set(head_info)
    hand, other = row_broadcast(jnp.concatenate([head_rows, info_rows], axis=0))
    is_even = row_index % 2 == 0
    first_pack = jnp.where(is_even, hand, other)
    second_pack = jnp.where(is_even, other, hand)
    heads = jnp.concatenate([first_pack[:block_width], second_pack[:block_width]], axis=0)
    info = jnp.concatenate(
        [first_pack[block_width : block_width + 4, :block_width],
         second_pack[block_width : block_width + 4, :block_width]],
        axis=1,
    )

    gram_11 = col_sum(times_transposed(heads[:block_width], heads[:block_width]))
    gram_2x = col_sum(times_transposed(heads[block_width:], heads))
    gram_21 = gram_2x[:, :block_width]
    gram_22 = gram_2x[:, block_width:]
    terms = times_transposed(local_rows, heads, lax.Precision.HIGH).reshape(
        col_count, row_share, 2 * block_width
    )
    sums = col_scatter(terms)

    first_coords = info[:3, :block_width]
    second_coords = info[:3, block_width:]
    first_diag = matern(first_coords, first_coords) - gram_11
    first_diag = first_diag + jnp.diag(info[3, :block_width])
    first_inverse = lower_inverse(first_diag)
    cross_rows = times_transposed(
        matern(second_coords, first_coords) - gram_21, first_inverse
    )
    second_diag = (
        matern(second_coords, second_coords)
        - gram_22
        - times_transposed(cross_rows, cross_rows)
    )
    second_diag = second_diag + jnp.diag(info[3, block_width:])
    second_inverse = lower_inverse(second_diag)

    first_cov = matern(my_coords, first_coords) - sums[:, :block_width]
    first_cov = first_cov.at[:block_width].add(jnp.where(first_owner, own_diag, 0.0))
    first_panel = times_transposed(first_cov, first_inverse)
    second_cov = (
        (matern(my_coords, second_coords) - sums[:, block_width:])
        - times_transposed(first_panel, cross_rows)
    )
    second_cov = second_cov.at[:block_width].add(jnp.where(second_owner, own_diag, 0.0))
    second_panel = times_transposed(second_cov, second_inverse)
    stacked = jnp.stack([first_panel, second_panel], axis=1)
    return stacked.reshape(1, 1, row_share, 2, block_width)


def solution(mesh):
    placed = (P(None, "row", None, None, "col", None), P(None, "row", None), P(None, "row", None))
    return jax.shard_map(
        body,
        mesh=mesh,
        in_specs=placed,
        out_specs=P("row", "col", None, None, None),
        check_vma=False,
    )
```

```python
import jax
import jax.numpy as jnp
from jax import lax
from jax.sharding import PartitionSpec as P

GRID_Y = 64
GRID_Z = 32


LATERAL = 24.0
VERTICAL = 6.0


def site_coords(site_ids):
    coord_x = site_ids // (GRID_Y * GRID_Z)
    coord_y = site_ids // GRID_Z % GRID_Y
    coord_z = site_ids % GRID_Z
    return jnp.stack([coord_x, coord_y, coord_z]).astype(jnp.float32)


def matern(row_coords, col_coords):
    lengths = (LATERAL, LATERAL, VERTICAL)
    squared = jnp.zeros((row_coords.shape[1], col_coords.shape[1]), jnp.float32)
    for dim_index in range(3):
        difference = (row_coords[dim_index][:, None] - col_coords[dim_index][None, :]) / lengths[
            dim_index
        ]
        squared = squared + difference * difference
    radius = jnp.sqrt(3.0 * squared)
    return (1.0 + radius) * jnp.exp(-radius)


def times_transposed(left_mat, right_mat, precision=lax.Precision.HIGHEST):
    return lax.dot_general(
        left_mat,
        right_mat,
        (((1,), (1,)), ((), ())),
        precision=precision,
        preferred_element_type=jnp.float32,
    )


def lower_inverse(square):
    factor = jnp.linalg.cholesky(square)
    return jax.scipy.linalg.solve_triangular(
        factor, jnp.eye(square.shape[0], dtype=jnp.float32), lower=True
    )


def col_sum(block):
    count = lax.axis_size("col")
    group = 1
    while group < count:
        width = min(4, count // group)
        parts = [
            lax.ppermute(block, "col", [(i, i ^ (k * group)) for i in range(count)])
            for k in range(1, width)
        ]
        for part in parts:
            block = block + part
        group *= width
    return block


def row_broadcast(pack):
    row = lax.axis_index("row")
    swap_home = lax.ppermute(pack, "row", [(0, 1), (1, 0)])
    first_out = lax.ppermute(pack, "row", [(0, 2), (1, 7)])
    relay = lax.ppermute(first_out, "row", [(2, 4), (7, 5)])
    second_out = lax.ppermute(
        jnp.where(row < 2, pack, first_out), "row", [(1, 3), (0, 6)]
    )
    hand = jnp.where(
        row < 2,
        pack,
        jnp.where((row == 2) | (row == 7), first_out, jnp.where((row == 4) | (row == 5), relay, second_out)),
    )
    swap_far = lax.ppermute(hand, "row", [(2, 3), (3, 2), (4, 5), (5, 4), (6, 7), (7, 6)])
    other = jnp.where(row < 2, swap_home, swap_far)
    return hand, other


def col_scatter(blocks):
    count = lax.axis_size("col")
    me = lax.axis_index("col")
    bits = count.bit_length() - 1
    shaped = blocks.reshape((2,) * bits + blocks.shape[1:])
    remaining = list(range(bits - 1, -1, -1))
    for bit in (1, 3, 0, 2)[:bits] if bits == 4 else range(bits):
        axis = remaining.index(bit)
        mine = (me >> bit) % 2
        keep = lax.dynamic_index_in_dim(shaped, mine, axis, keepdims=False)
        send = lax.dynamic_index_in_dim(shaped, 1 - mine, axis, keepdims=False)
        shaped = keep + lax.ppermute(send, "col", [(i, i ^ (1 << bit)) for i in range(count)])
        remaining.pop(axis)
    return shaped


def body(left_factor, pick_site, noise):
    row_blocks, _, block_width, col_blocks, _, _ = left_factor.shape
    col_count = lax.axis_size("col")
    row_share = row_blocks * block_width // col_count
    row_index = lax.axis_index("row")
    col_index = lax.axis_index("col")
    local_rows = left_factor.reshape(row_blocks * block_width, col_blocks * block_width)
    site_flat = pick_site.reshape(row_blocks * block_width)
    noise_flat = noise.reshape(row_blocks * block_width)
    offset = col_index * row_share
    my_coords = site_coords(lax.dynamic_slice_in_dim(site_flat, offset, row_share))
    my_noise = lax.dynamic_slice_in_dim(noise_flat, offset, row_share)
    first_owner = (row_index == 0) & (col_index == 0)
    second_owner = (row_index == 1) & (col_index == 0)
    own_diag = jnp.diag(my_noise[:block_width])

    head_rows = local_rows[:block_width]
    head_info = jnp.concatenate(
        [site_coords(site_flat[:block_width]), noise_flat[None, :block_width]], axis=0
    )
    is_first = row_index == 0
    is_second = row_index == 1
    info_rows = jnp.zeros((8, head_rows.shape[1]), jnp.float32).at[:4, :block_width].set(head_info)
    hand, other = row_broadcast(jnp.concatenate([head_rows, info_rows], axis=0))
    is_even = row_index % 2 == 0
    first_pack = jnp.where(is_even, hand, other)
    second_pack = jnp.where(is_even, other, hand)
    heads = jnp.concatenate([first_pack[:block_width], second_pack[:block_width]], axis=0)
    info = jnp.concatenate(
        [first_pack[block_width : block_width + 4, :block_width],
         second_pack[block_width : block_width + 4, :block_width]],
        axis=1,
    )

    gram_11 = col_sum(times_transposed(heads[:block_width], heads[:block_width]))
    gram_2x = col_sum(times_transposed(heads[block_width:], heads))
    gram_21 = gram_2x[:, :block_width]
    gram_22 = gram_2x[:, block_width:]
    terms = times_transposed(local_rows, heads, lax.Precision.HIGH).reshape(
        col_count, row_share, 2 * block_width
    )
    sums = col_scatter(terms)

    first_coords = info[:3, :block_width]
    second_coords = info[:3, block_width:]
    first_diag = matern(first_coords, first_coords) - gram_11
    first_diag = first_diag + jnp.diag(info[3, :block_width])
    first_inverse = lower_inverse(first_diag)
    cross_rows = times_transposed(
        matern(second_coords, first_coords) - gram_21, first_inverse
    )
    second_diag = (
        matern(second_coords, second_coords)
        - gram_22
        - times_transposed(cross_rows, cross_rows)
    )
    second_diag = second_diag + jnp.diag(info[3, block_width:])
    second_inverse = lower_inverse(second_diag)

    first_cov = matern(my_coords, first_coords) - sums[:, :block_width]
    first_cov = first_cov.at[:block_width].add(jnp.where(first_owner, own_diag, 0.0))
    first_panel = times_transposed(first_cov, first_inverse)
    second_cov = (
        (matern(my_coords, second_coords) - sums[:, block_width:])
        - times_transposed(first_panel, cross_rows)
    )
    second_cov = second_cov.at[:block_width].add(jnp.where(second_owner, own_diag, 0.0))
    second_panel = times_transposed(second_cov, second_inverse)
    stacked = jnp.stack([first_panel, second_panel], axis=1)
    return stacked.reshape(1, 1, row_share, 2, block_width)


def solution(mesh):
    placed = (P(None, "row", None, None, "col", None), P(None, "row", None), P(None, "row", None))
    return jax.shard_map(
        body,
        mesh=mesh,
        in_specs=placed,
        out_specs=P("row", "col", None, None, None),
        check_vma=False,
    )
```

```python
import jax
import jax.numpy as jnp
from jax import lax
from jax.sharding import PartitionSpec as P

GRID_Y = 64
GRID_Z = 32


LATERAL = 24.0
VERTICAL = 6.0


def site_coords(site_ids):
    coord_x = site_ids // (GRID_Y * GRID_Z)
    coord_y = site_ids // GRID_Z % GRID_Y
    coord_z = site_ids % GRID_Z
    return jnp.stack([coord_x, coord_y, coord_z]).astype(jnp.float32)


def matern(row_coords, col_coords):
    lengths = (LATERAL, LATERAL, VERTICAL)
    squared = jnp.zeros((row_coords.shape[1], col_coords.shape[1]), jnp.float32)
    for dim_index in range(3):
        difference = (row_coords[dim_index][:, None] - col_coords[dim_index][None, :]) / lengths[
            dim_index
        ]
        squared = squared + difference * difference
    radius = jnp.sqrt(3.0 * squared)
    return (1.0 + radius) * jnp.exp(-radius)


def times_transposed(left_mat, right_mat, precision=lax.Precision.HIGHEST):
    return lax.dot_general(
        left_mat,
        right_mat,
        (((1,), (1,)), ((), ())),
        precision=precision,
        preferred_element_type=jnp.float32,
    )


def lower_inverse(square):
    factor = jnp.linalg.cholesky(square)
    return jax.scipy.linalg.solve_triangular(
        factor, jnp.eye(square.shape[0], dtype=jnp.float32), lower=True
    )


def col_sum(block):
    count = lax.axis_size("col")
    group = 1
    while group < count:
        width = min(4, count // group)
        parts = [
            lax.ppermute(block, "col", [(i, i ^ (k * group)) for i in range(count)])
            for k in range(1, width)
        ]
        for part in parts:
            block = block + part
        group *= width
    return block


def row_broadcast(pack):
    row = lax.axis_index("row")
    swap_home = lax.ppermute(pack, "row", [(0, 1), (1, 0)])
    first_out = lax.ppermute(pack, "row", [(0, 2), (1, 7)])
    relay = lax.ppermute(first_out, "row", [(2, 4), (7, 5)])
    second_out = lax.ppermute(
        jnp.where(row < 2, pack, first_out), "row", [(1, 3), (0, 6)]
    )
    hand = jnp.where(
        row < 2,
        pack,
        jnp.where((row == 2) | (row == 7), first_out, jnp.where((row == 4) | (row == 5), relay, second_out)),
    )
    swap_far = lax.ppermute(hand, "row", [(2, 3), (3, 2), (4, 5), (5, 4), (6, 7), (7, 6)])
    other = jnp.where(row < 2, swap_home, swap_far)
    return hand, other


def col_scatter(blocks):
    count = lax.axis_size("col")
    me = lax.axis_index("col")
    ring = 4
    order = [0, 3, 1, 2]
    shaped = blocks.reshape((ring, ring) + blocks.shape[1:])
    shaped = jnp.stack([shaped[z] for z in order])
    shaped = jnp.stack([shaped[:, y] for y in order], axis=1)
    shaped = shaped.reshape((2, 2, 2, 2) + blocks.shape[1:])
    my_z, my_y = me // ring, me % ring

    def pairs(step_of):
        return [(z * ring + y, step_of(z, y)) for z in range(ring) for y in range(ring)]

    steps = (
        (2, (my_y ^ (my_y >> 1)) % 2, pairs(lambda z, y: z * ring + (y ^ 1))),
        (0, (my_z ^ (my_z >> 1)) % 2, pairs(lambda z, y: (z ^ 1) * ring + y)),
        (1, my_y >> 1, pairs(lambda z, y: z * ring + (ring - 1 - y))),
        (0, my_z >> 1, pairs(lambda z, y: (ring - 1 - z) * ring + y)),
    )
    for axis, mine, perm in steps:
        keep = lax.dynamic_index_in_dim(shaped, mine, axis, keepdims=False)
        send = lax.dynamic_index_in_dim(shaped, 1 - mine, axis, keepdims=False)
        shaped = keep + lax.ppermute(send, "col", perm)
    return shaped


def body(left_factor, pick_site, noise):
    row_blocks, _, block_width, col_blocks, _, _ = left_factor.shape
    col_count = lax.axis_size("col")
    row_share = row_blocks * block_width // col_count
    row_index = lax.axis_index("row")
    col_index = lax.axis_index("col")
    local_rows = left_factor.reshape(row_blocks * block_width, col_blocks * block_width)
    site_flat = pick_site.reshape(row_blocks * block_width)
    noise_flat = noise.reshape(row_blocks * block_width)
    offset = col_index * row_share
    my_coords = site_coords(lax.dynamic_slice_in_dim(site_flat, offset, row_share))
    my_noise = lax.dynamic_slice_in_dim(noise_flat, offset, row_share)
    first_owner = (row_index == 0) & (col_index == 0)
    second_owner = (row_index == 1) & (col_index == 0)
    own_diag = jnp.diag(my_noise[:block_width])

    head_rows = local_rows[:block_width]
    head_info = jnp.concatenate(
        [site_coords(site_flat[:block_width]), noise_flat[None, :block_width]], axis=0
    )
    is_first = row_index == 0
    is_second = row_index == 1
    info_rows = jnp.zeros((8, head_rows.shape[1]), jnp.float32).at[:4, :block_width].set(head_info)
    hand, other = row_broadcast(jnp.concatenate([head_rows, info_rows], axis=0))
    is_even = row_index % 2 == 0
    first_pack = jnp.where(is_even, hand, other)
    second_pack = jnp.where(is_even, other, hand)
    heads = jnp.concatenate([first_pack[:block_width], second_pack[:block_width]], axis=0)
    info = jnp.concatenate(
        [first_pack[block_width : block_width + 4, :block_width],
         second_pack[block_width : block_width + 4, :block_width]],
        axis=1,
    )

    gram_11 = col_sum(times_transposed(heads[:block_width], heads[:block_width]))
    gram_2x = col_sum(times_transposed(heads[block_width:], heads))
    gram_21 = gram_2x[:, :block_width]
    gram_22 = gram_2x[:, block_width:]
    terms = times_transposed(local_rows, heads, lax.Precision.HIGH).reshape(
        col_count, row_share, 2 * block_width
    )
    sums = col_scatter(terms)

    first_coords = info[:3, :block_width]
    second_coords = info[:3, block_width:]
    first_diag = matern(first_coords, first_coords) - gram_11
    first_diag = first_diag + jnp.diag(info[3, :block_width])
    first_inverse = lower_inverse(first_diag)
    cross_rows = times_transposed(
        matern(second_coords, first_coords) - gram_21, first_inverse
    )
    second_diag = (
        matern(second_coords, second_coords)
        - gram_22
        - times_transposed(cross_rows, cross_rows)
    )
    second_diag = second_diag + jnp.diag(info[3, block_width:])
    second_inverse = lower_inverse(second_diag)

    first_cov = matern(my_coords, first_coords) - sums[:, :block_width]
    first_cov = first_cov.at[:block_width].add(jnp.where(first_owner, own_diag, 0.0))
    first_panel = times_transposed(first_cov, first_inverse)
    second_cov = (
        (matern(my_coords, second_coords) - sums[:, block_width:])
        - times_transposed(first_panel, cross_rows)
    )
    second_cov = second_cov.at[:block_width].add(jnp.where(second_owner, own_diag, 0.0))
    second_panel = times_transposed(second_cov, second_inverse)
    stacked = jnp.stack([first_panel, second_panel], axis=1)
    return stacked.reshape(1, 1, row_share, 2, block_width)


def solution(mesh):
    placed = (P(None, "row", None, None, "col", None), P(None, "row", None), P(None, "row", None))
    return jax.shard_map(
        body,
        mesh=mesh,
        in_specs=placed,
        out_specs=P("row", "col", None, None, None),
        check_vma=False,
    )
```

```python
import jax
import jax.numpy as jnp
from jax import lax
from jax.sharding import PartitionSpec as P

GRID_Y = 64
GRID_Z = 32


LATERAL = 24.0
VERTICAL = 6.0


def site_coords(site_ids):
    coord_x = site_ids // (GRID_Y * GRID_Z)
    coord_y = site_ids // GRID_Z % GRID_Y
    coord_z = site_ids % GRID_Z
    return jnp.stack([coord_x, coord_y, coord_z]).astype(jnp.float32)


def matern(row_coords, col_coords):
    lengths = (LATERAL, LATERAL, VERTICAL)
    squared = jnp.zeros((row_coords.shape[1], col_coords.shape[1]), jnp.float32)
    for dim_index in range(3):
        difference = (row_coords[dim_index][:, None] - col_coords[dim_index][None, :]) / lengths[
            dim_index
        ]
        squared = squared + difference * difference
    radius = jnp.sqrt(3.0 * squared)
    return (1.0 + radius) * jnp.exp(-radius)


def times_transposed(left_mat, right_mat, precision=lax.Precision.HIGHEST):
    return lax.dot_general(
        left_mat,
        right_mat,
        (((1,), (1,)), ((), ())),
        precision=precision,
        preferred_element_type=jnp.float32,
    )


def lower_inverse(square):
    factor = jnp.linalg.cholesky(square)
    return jax.scipy.linalg.solve_triangular(
        factor, jnp.eye(square.shape[0], dtype=jnp.float32), lower=True
    )


def col_sum(block):
    count = lax.axis_size("col")
    group = 1
    while group < count:
        width = min(4, count // group)
        parts = [
            lax.ppermute(block, "col", [(i, i ^ (k * group)) for i in range(count)])
            for k in range(1, width)
        ]
        for part in parts:
            block = block + part
        group *= width
    return block


def row_broadcast(pack):
    row = lax.axis_index("row")
    swap_home = lax.ppermute(pack, "row", [(0, 1), (1, 0)])
    first_out = lax.ppermute(pack, "row", [(0, 2), (1, 7)])
    relay = lax.ppermute(first_out, "row", [(2, 4), (7, 5)])
    second_out = lax.ppermute(
        jnp.where(row < 2, pack, first_out), "row", [(1, 3), (0, 6)]
    )
    hand = jnp.where(
        row < 2,
        pack,
        jnp.where((row == 2) | (row == 7), first_out, jnp.where((row == 4) | (row == 5), relay, second_out)),
    )
    swap_far = lax.ppermute(hand, "row", [(2, 3), (3, 2), (4, 5), (5, 4), (6, 7), (7, 6)])
    other = jnp.where(row < 2, swap_home, swap_far)
    return hand, other


def col_scatter(blocks):
    count = lax.axis_size("col")
    me = lax.axis_index("col")
    ring = 4
    order = [0, 3, 1, 2]
    shaped = blocks.reshape((ring, ring) + blocks.shape[1:])
    shaped = jnp.stack([shaped[z] for z in order])
    shaped = jnp.stack([shaped[:, y] for y in order], axis=1)
    shaped = shaped.reshape((2, 2, 2, 2) + blocks.shape[1:])
    my_z, my_y = me // ring, me % ring

    def pairs(step_of):
        return [(z * ring + y, step_of(z, y)) for z in range(ring) for y in range(ring)]

    steps = (
        (2, (my_y ^ (my_y >> 1)) % 2, pairs(lambda z, y: z * ring + (y ^ 1))),
        (0, (my_z ^ (my_z >> 1)) % 2, pairs(lambda z, y: (z ^ 1) * ring + y)),
        (1, my_y >> 1, pairs(lambda z, y: z * ring + (ring - 1 - y))),
        (0, my_z >> 1, pairs(lambda z, y: (ring - 1 - z) * ring + y)),
    )
    for axis, mine, perm in steps[:-1]:
        keep = lax.dynamic_index_in_dim(shaped, mine, axis, keepdims=False)
        send = lax.dynamic_index_in_dim(shaped, 1 - mine, axis, keepdims=False)
        shaped = keep + lax.ppermute(send, "col", perm)
    axis, mine, perm = steps[-1]
    keep = lax.dynamic_index_in_dim(shaped, mine, axis, keepdims=False)
    send = lax.dynamic_index_in_dim(shaped, 1 - mine, axis, keepdims=False)
    cut = send.shape[-1] // 2
    first = keep[..., :cut] + lax.ppermute(send[..., :cut], "col", perm)
    second = keep[..., cut:] + lax.ppermute(send[..., cut:], "col", perm)
    return first, second


def body(left_factor, pick_site, noise):
    row_blocks, _, block_width, col_blocks, _, _ = left_factor.shape
    col_count = lax.axis_size("col")
    row_share = row_blocks * block_width // col_count
    row_index = lax.axis_index("row")
    col_index = lax.axis_index("col")
    local_rows = left_factor.reshape(row_blocks * block_width, col_blocks * block_width)
    site_flat = pick_site.reshape(row_blocks * block_width)
    noise_flat = noise.reshape(row_blocks * block_width)
    offset = col_index * row_share
    my_coords = site_coords(lax.dynamic_slice_in_dim(site_flat, offset, row_share))
    my_noise = lax.dynamic_slice_in_dim(noise_flat, offset, row_share)
    first_owner = (row_index == 0) & (col_index == 0)
    second_owner = (row_index == 1) & (col_index == 0)
    own_diag = jnp.diag(my_noise[:block_width])

    head_rows = local_rows[:block_width]
    head_info = jnp.concatenate(
        [site_coords(site_flat[:block_width]), noise_flat[None, :block_width]], axis=0
    )
    is_first = row_index == 0
    is_second = row_index == 1
    info_rows = jnp.zeros((8, head_rows.shape[1]), jnp.float32).at[:4, :block_width].set(head_info)
    hand, other = row_broadcast(jnp.concatenate([head_rows, info_rows], axis=0))
    is_even = row_index % 2 == 0
    first_pack = jnp.where(is_even, hand, other)
    second_pack = jnp.where(is_even, other, hand)
    heads = jnp.concatenate([first_pack[:block_width], second_pack[:block_width]], axis=0)
    info = jnp.concatenate(
        [first_pack[block_width : block_width + 4, :block_width],
         second_pack[block_width : block_width + 4, :block_width]],
        axis=1,
    )

    gram_11 = col_sum(times_transposed(heads[:block_width], heads[:block_width]))
    gram_2x = col_sum(times_transposed(heads[block_width:], heads))
    gram_21 = gram_2x[:, :block_width]
    gram_22 = gram_2x[:, block_width:]
    terms = times_transposed(local_rows, heads, lax.Precision.HIGH).reshape(
        col_count, row_share, 2 * block_width
    )
    first_sums, second_sums = col_scatter(terms)

    first_coords = info[:3, :block_width]
    second_coords = info[:3, block_width:]
    first_diag = matern(first_coords, first_coords) - gram_11
    first_diag = first_diag + jnp.diag(info[3, :block_width])
    first_inverse = lower_inverse(first_diag)
    cross_rows = times_transposed(
        matern(second_coords, first_coords) - gram_21, first_inverse
    )
    second_diag = (
        matern(second_coords, second_coords)
        - gram_22
        - times_transposed(cross_rows, cross_rows)
    )
    second_diag = second_diag + jnp.diag(info[3, block_width:])
    second_inverse = lower_inverse(second_diag)

    first_cov = matern(my_coords, first_coords) - first_sums
    first_cov = first_cov.at[:block_width].add(jnp.where(first_owner, own_diag, 0.0))
    first_panel = times_transposed(first_cov, first_inverse)
    second_cov = (
        (matern(my_coords, second_coords) - second_sums)
        - times_transposed(first_panel, cross_rows)
    )
    second_cov = second_cov.at[:block_width].add(jnp.where(second_owner, own_diag, 0.0))
    second_panel = times_transposed(second_cov, second_inverse)
    stacked = jnp.stack([first_panel, second_panel], axis=1)
    return stacked.reshape(1, 1, row_share, 2, block_width)


def solution(mesh):
    placed = (P(None, "row", None, None, "col", None), P(None, "row", None), P(None, "row", None))
    return jax.shard_map(
        body,
        mesh=mesh,
        in_specs=placed,
        out_specs=P("row", "col", None, None, None),
        check_vma=False,
    )
```

```python
import jax
import jax.numpy as jnp
from jax import lax
from jax.sharding import PartitionSpec as P

GRID_Y = 64
GRID_Z = 32


LATERAL = 24.0
VERTICAL = 6.0


def site_coords(site_ids):
    coord_x = site_ids // (GRID_Y * GRID_Z)
    coord_y = site_ids // GRID_Z % GRID_Y
    coord_z = site_ids % GRID_Z
    return jnp.stack([coord_x, coord_y, coord_z]).astype(jnp.float32)


def matern(row_coords, col_coords):
    lengths = (LATERAL, LATERAL, VERTICAL)
    squared = jnp.zeros((row_coords.shape[1], col_coords.shape[1]), jnp.float32)
    for dim_index in range(3):
        difference = (row_coords[dim_index][:, None] - col_coords[dim_index][None, :]) / lengths[
            dim_index
        ]
        squared = squared + difference * difference
    radius = jnp.sqrt(3.0 * squared)
    return (1.0 + radius) * jnp.exp(-radius)


def times_transposed(left_mat, right_mat, precision=lax.Precision.HIGHEST):
    return lax.dot_general(
        left_mat,
        right_mat,
        (((1,), (1,)), ((), ())),
        precision=precision,
        preferred_element_type=jnp.float32,
    )


def lower_inverse(square):
    factor = jnp.linalg.cholesky(square)
    return jax.scipy.linalg.solve_triangular(
        factor, jnp.eye(square.shape[0], dtype=jnp.float32), lower=True
    )


def col_sum(block):
    count = lax.axis_size("col")
    group = 1
    while group < count:
        width = min(4, count // group)
        parts = [
            lax.ppermute(block, "col", [(i, i ^ (k * group)) for i in range(count)])
            for k in range(1, width)
        ]
        for part in parts:
            block = block + part
        group *= width
    return block


def row_broadcast(pack):
    row = lax.axis_index("row")
    swap_home = lax.ppermute(pack, "row", [(0, 1), (1, 0)])
    first_out = lax.ppermute(pack, "row", [(0, 2), (1, 7)])
    relay = lax.ppermute(first_out, "row", [(2, 4), (7, 5)])
    second_out = lax.ppermute(
        jnp.where(row < 2, pack, first_out), "row", [(1, 3), (0, 6)]
    )
    hand = jnp.where(
        row < 2,
        pack,
        jnp.where((row == 2) | (row == 7), first_out, jnp.where((row == 4) | (row == 5), relay, second_out)),
    )
    swap_far = lax.ppermute(hand, "row", [(2, 3), (3, 2), (4, 5), (5, 4), (6, 7), (7, 6)])
    other = jnp.where(row < 2, swap_home, swap_far)
    return hand, other


def col_scatter(blocks):
    count = lax.axis_size("col")
    me = lax.axis_index("col")
    ring = 4
    order = [0, 3, 1, 2]
    shaped = blocks.reshape((ring, ring) + blocks.shape[1:])
    shaped = jnp.stack([shaped[z] for z in order])
    shaped = jnp.stack([shaped[:, y] for y in order], axis=1)
    shaped = shaped.reshape((2, 2, 2, 2) + blocks.shape[1:])
    my_z, my_y = me // ring, me % ring

    def pairs(step_of):
        return [(z * ring + y, step_of(z, y)) for z in range(ring) for y in range(ring)]

    steps = (
        (2, (my_y ^ (my_y >> 1)) % 2, pairs(lambda z, y: z * ring + (y ^ 1))),
        (0, (my_z ^ (my_z >> 1)) % 2, pairs(lambda z, y: (z ^ 1) * ring + y)),
        (1, my_y >> 1, pairs(lambda z, y: z * ring + (ring - 1 - y))),
        (0, my_z >> 1, pairs(lambda z, y: (ring - 1 - z) * ring + y)),
    )
    for axis, mine, perm in steps:
        keep = lax.dynamic_index_in_dim(shaped, mine, axis, keepdims=False)
        send = lax.dynamic_index_in_dim(shaped, 1 - mine, axis, keepdims=False)
        shaped = keep + lax.ppermute(send, "col", perm)
    return shaped


def body(left_factor, pick_site, noise):
    row_blocks, _, block_width, col_blocks, _, _ = left_factor.shape
    col_count = lax.axis_size("col")
    row_share = row_blocks * block_width // col_count
    row_index = lax.axis_index("row")
    col_index = lax.axis_index("col")
    local_rows = left_factor.reshape(row_blocks * block_width, col_blocks * block_width)
    site_flat = pick_site.reshape(row_blocks * block_width)
    noise_flat = noise.reshape(row_blocks * block_width)
    offset = col_index * row_share
    my_coords = site_coords(lax.dynamic_slice_in_dim(site_flat, offset, row_share))
    my_noise = lax.dynamic_slice_in_dim(noise_flat, offset, row_share)
    first_owner = (row_index == 0) & (col_index == 0)
    second_owner = (row_index == 1) & (col_index == 0)
    own_diag = jnp.diag(my_noise[:block_width])

    head_rows = local_rows[:block_width]
    head_info = jnp.concatenate(
        [site_coords(site_flat[:block_width]), noise_flat[None, :block_width]], axis=0
    )
    is_first = row_index == 0
    is_second = row_index == 1
    head_flat = left_factor[0, 0].reshape(block_width * col_blocks, block_width)
    info_rows = jnp.zeros((8, block_width), jnp.float32).at[:4].set(head_info)
    hand, other = row_broadcast(jnp.concatenate([head_flat, info_rows], axis=0))
    is_even = row_index % 2 == 0
    first_pack = jnp.where(is_even, hand, other)
    second_pack = jnp.where(is_even, other, hand)
    flat_rows = block_width * col_blocks
    heads = jnp.concatenate(
        [first_pack[:flat_rows].reshape(block_width, -1), second_pack[:flat_rows].reshape(block_width, -1)],
        axis=0,
    )
    info = jnp.concatenate(
        [first_pack[flat_rows : flat_rows + 4], second_pack[flat_rows : flat_rows + 4]], axis=1
    )

    gram_11 = col_sum(times_transposed(heads[:block_width], heads[:block_width]))
    gram_2x = col_sum(times_transposed(heads[block_width:], heads))
    gram_21 = gram_2x[:, :block_width]
    gram_22 = gram_2x[:, block_width:]
    terms = times_transposed(local_rows, heads, lax.Precision.HIGH).reshape(
        col_count, row_share, 2 * block_width
    )
    sums = col_scatter(terms)

    first_coords = info[:3, :block_width]
    second_coords = info[:3, block_width:]
    first_diag = matern(first_coords, first_coords) - gram_11
    first_diag = first_diag + jnp.diag(info[3, :block_width])
    first_inverse = lower_inverse(first_diag)
    cross_rows = times_transposed(
        matern(second_coords, first_coords) - gram_21, first_inverse
    )
    second_diag = (
        matern(second_coords, second_coords)
        - gram_22
        - times_transposed(cross_rows, cross_rows)
    )
    second_diag = second_diag + jnp.diag(info[3, block_width:])
    second_inverse = lower_inverse(second_diag)

    first_cov = matern(my_coords, first_coords) - sums[:, :block_width]
    first_cov = first_cov.at[:block_width].add(jnp.where(first_owner, own_diag, 0.0))
    first_panel = times_transposed(first_cov, first_inverse)
    second_cov = (
        (matern(my_coords, second_coords) - sums[:, block_width:])
        - times_transposed(first_panel, cross_rows)
    )
    second_cov = second_cov.at[:block_width].add(jnp.where(second_owner, own_diag, 0.0))
    second_panel = times_transposed(second_cov, second_inverse)
    stacked = jnp.stack([first_panel, second_panel], axis=1)
    return stacked.reshape(1, 1, row_share, 2, block_width)


def solution(mesh):
    placed = (P(None, "row", None, None, "col", None), P(None, "row", None), P(None, "row", None))
    return jax.shard_map(
        body,
        mesh=mesh,
        in_specs=placed,
        out_specs=P("row", "col", None, None, None),
        check_vma=False,
    )
```
